512 devices in a mesh: lat: 8 (over y_lo, core), lon: 64 (over x, y_hi, z).
Axes of the slice: x: 4, y: 8 (y_hi: 2, y_lo: 4; y = y_hi * 4 + y_lo), z: 8, core: 2. Of those that a mesh axis runs over, the one named last changes fastest.
Arguments:
- fields: bfloat16 [512, 1024, 256], P('lat', 'lon'), may hold values from -16 to 16
- kernel: bfloat16 [3, 3, 256, 256], replicated, may hold values from -0.125 to 0.125
- norm_gain: float32 [256], replicated, may hold values from 0.5 to 1.5
- norm_shift: float32 [256], replicated, may hold values from -3 to 3
- cotangent: bfloat16 [512, 1024, 256], P('lat', 'lon'), may hold values from -6 to 6
Outputs:
- block_out: bfloat16 [512, 1024, 256], P('lat', 'lon')
- grad_fields: bfloat16 [512, 1024, 256], P('lat', 'lon')
- grad_kernel: float32 [2304, 256], P('lon', 'lat')
- grad_gain: float32 [256], replicated
- grad_shift: float32 [256], replicated
The draws below stay inside these ranges and needn't reach their ends.
All inputs are finite; a program needn't handle non-finite values.
Results may differ from the reference program's by a relative error of at most 0.004.
Values may be sent and summed in bfloat16 or wider, within the bound.
No kernel may reach another device: no remote copies, remote signals or barrier semaphores. Data moves between devices by JAX's collectives and lax.ppermute only.
A program may use at most 64 MiB of HBM per device.

```python
import math
import jax
import jax.numpy as jnp
from jax import lax

C = 256
G = 32
NLAT = 512
NLON = 1024


def draw_fields(key, part):
    keys = jax.random.split(key, 4)
    lat_pos = jnp.arange(NLAT, dtype=jnp.float32) / NLAT
    lon_pos = jnp.arange(NLON, dtype=jnp.float32) / NLON
    row_scale = (1.0 + 2.0 * lat_pos) * jnp.exp(jax.random.uniform(keys[1], (NLAT,), jnp.float32, 0.0, math.log(1.7)))
    col_scale = (1.0 + 2.0 * lon_pos) * jnp.exp(jax.random.uniform(keys[2], (NLON,), jnp.float32, 0.0, math.log(1.7)))
    chan_scale = jnp.exp(jax.random.uniform(keys[3], (C,), jnp.float32, math.log(0.5), math.log(2.0)))
    base = jnp.clip(jax.random.normal(keys[0], (NLAT, NLON, C), jnp.float32), -4.0, 4.0)
    values = 0.06 * base * row_scale[:, None, None] * col_scale[None, :, None] * chan_scale[None, None, :]
    return values.astype(jnp.bfloat16)


def level_of(rng, dims, cuts, low, top_value):
    level, own = 1.0, jax.random.fold_in(rng, 6)
    for axis_at, shards_of in cuts:
        draws = jnp.exp(jax.random.uniform(jax.random.fold_in(own, axis_at), (shards_of,), jnp.float32, low / len(cuts), top_value / len(cuts)))
        level = level * jnp.repeat(draws, dims[axis_at] // shards_of).reshape([-1 if axis == axis_at else 1 for axis in range(len(dims))])
    return level


def centred(own_key, dims, scale, bound, cuts=(), kind=jnp.bfloat16):
    entries = jax.random.normal(own_key, dims, jnp.float32) * scale
    if len(cuts) > 0:
        entries = level_of(own_key, dims, cuts, -0.22, 0.18) * entries
    return jnp.clip(entries, min=-bound, max=bound).astype(kind)


def setup_inputs(seed: int = 0) -> dict:
    key_list = jax.random.split(jax.random.key(seed), 6)
    return {
        "fields": draw_fields(jax.random.fold_in(key_list[5], 71), 0),
        "kernel": centred(key_list[1], (3, 3, C, C), (9 * C) ** -0.5, 0.125),
        "norm_gain": jnp.clip(1.0 + 0.1 * jax.random.normal(key_list[2], (C,), jnp.float32), 0.5, 1.5),
        "norm_shift": centred(key_list[3], (C,), 0.5, 3.0, (), jnp.float32),
        "cotangent": centred(key_list[4], (NLAT, NLON, C), 1.0, 6.0, ((0, 8), (1, 64))),
    }


def extend_grid(field):
    halfway = NLON // 2
    upper = jnp.roll(field[0], -halfway, axis=0)
    lower = jnp.roll(field[-1], -halfway, axis=0)
    banded = jnp.concatenate([upper[None], field, lower[None]], 0)
    return jnp.concatenate([banded[:, -1:], banded, banded[:, :1]], 1)

def convolve(field, weights):
    padded = extend_grid(field)
    total = jnp.zeros((NLAT * NLON, C), jnp.float32)
    for tap_row in range(3):
        for tap_col in range(3):
            window = padded[tap_row:tap_row + NLAT, tap_col:tap_col + NLON].reshape(-1, C)
            total = total + jnp.dot(window, weights[tap_row, tap_col], preferred_element_type=jnp.float32)
    return total

def reference(fields, kernel, norm_gain, norm_shift, cotangent):
    inputs = fields.astype(jnp.float32)
    weights = kernel.astype(jnp.float32)
    conv_out = convolve(inputs, weights)
    count = NLAT * NLON * (C // G)
    first = lax.optimization_barrier(jnp.sum(conv_out, 0))
    second = lax.optimization_barrier(jnp.sum(conv_out * conv_out, 0))
    mean = first.reshape(G, -1).sum(1) / count
    var = second.reshape(G, -1).sum(1) / count - mean * mean
    rstd = lax.rsqrt(var + 1e-05)
    mean_ch = jnp.repeat(mean, C // G)
    rstd_ch = jnp.repeat(rstd, C // G)
    ghat = (conv_out - mean_ch) * rstd_ch
    pre = ghat * norm_gain + norm_shift
    sigma = jax.nn.sigmoid(pre)
    block_out = (inputs.reshape(-1, C) + pre * sigma).astype(jnp.bfloat16).reshape(NLAT, NLON, C)
    upstream = cotangent.astype(jnp.float32).reshape(-1, C)
    dpre = upstream * (sigma * (1.0 + pre * (1.0 - sigma)))
    grad_gain = lax.optimization_barrier(jnp.sum(dpre * ghat, 0))
    grad_shift = lax.optimization_barrier(jnp.sum(dpre, 0))
    mean_a = (norm_gain * grad_shift).reshape(G, -1).sum(1) / count
    mean_b = (norm_gain * grad_gain).reshape(G, -1).sum(1) / count
    dconv = ((dpre * norm_gain - jnp.repeat(mean_a, C // G) - ghat * jnp.repeat(mean_b, C // G)) * rstd_ch).astype(jnp.bfloat16)
    dconv_f = dconv.astype(jnp.float32)
    primal, pullback = jax.vjp(lambda value: convolve(value, weights), inputs)
    back = pullback(dconv_f)[0]
    grad_fields = (upstream.reshape(NLAT, NLON, C) + back).astype(jnp.bfloat16)
    padded = extend_grid(inputs)
    pieces = []
    for tap_row in range(3):
        for tap_col in range(3):
            window = padded[tap_row:tap_row + NLAT, tap_col:tap_col + NLON].reshape(-1, C)
            pieces.append(lax.dot_general(window, dconv_f, (((0,), (0,)), ((), ())), preferred_element_type=jnp.float32))
    grad_kernel = jnp.concatenate(pieces, 0)
    return (block_out, grad_fields, grad_kernel, grad_gain, grad_shift)
```

```python
import jax
import jax.numpy as jnp
from jax import lax
from jax.sharding import PartitionSpec as P

G = 32


def with_halo(shard, sides, width, wrap):
    for axis, dim in sides:
        peers, length = (lax.axis_size(axis), shard.shape[dim])
        up = [(i, (i + 1) % peers) for i in range(peers if wrap else peers - 1)]
        down = [(j, i) for i, j in up]
        last = lax.slice_in_dim(shard, length - width, length, axis=dim)
        initial = lax.slice_in_dim(shard, 0, width, axis=dim)
        before = lax.ppermute(last, axis, up)
        after = lax.ppermute(initial, axis, down)
        shard = jnp.concatenate([before, shard, after], axis=dim)
    return shard


def passed_along(block, axis, distance):
    devices = range(lax.axis_size(axis))
    route = [((i - distance) % len(devices), i) for i in devices]
    return lax.ppermute(block, axis, route)


def extend(field):
    halfway = lax.axis_size("lon") // 2
    widened = with_halo(field, (("lon", 1),), 1, True)
    banded = with_halo(widened, (("lat", 0),), 1, False)
    distant = passed_along(jnp.stack([widened[0], widened[-1]]), "lon", halfway)
    return (banded, distant)


def exchange(block, axis, bit):
    peers = lax.axis_size(axis)
    return lax.ppermute(block, axis, [(i, i ^ (1 << bit)) for i in range(peers)])


def butterfly_order():
    lat_bits = (lax.axis_size("lat") - 1).bit_length()
    lon_bits = (lax.axis_size("lon") - 1).bit_length()
    order = [("lat", b) for b in range(lat_bits)] + [("lon", b) for b in range(lon_bits)]
    return order


def butterfly_sum(value):
    for axis, bit in butterfly_order():
        value = value + exchange(value, axis, bit)
    return value


def halving_sum(blocks):
    lat_n, lon_n = blocks.shape[0], blocks.shape[1]
    lat_bits, lon_bits = (lat_n - 1).bit_length(), (lon_n - 1).bit_length()
    tail = blocks.shape[2:]
    split = blocks.reshape((2,) * lat_bits + (2,) * lon_bits + tail)
    dims = {("lat", b): lat_bits - 1 - b for b in range(lat_bits)}
    dims.update({("lon", b): lat_bits + lon_bits - 1 - b for b in range(lon_bits)})
    for axis, bit in butterfly_order():
        dim = dims[(axis, bit)]
        mine = (lax.axis_index(axis) >> bit) & 1
        keep = lax.dynamic_index_in_dim(split, mine, dim, keepdims=False)
        send = lax.dynamic_index_in_dim(split, 1 - mine, dim, keepdims=False)
        split = keep + exchange(send, axis, bit)
        dims = {k: (d - 1 if d > dim else d) for k, d in dims.items() if k != (axis, bit)}
    return split.reshape(tail)


def local(fields, kernel, norm_gain, norm_shift, cotangent):
    height, breadth, channels = fields.shape
    north = lax.axis_index("lat") == 0
    south = lax.axis_index("lat") == lax.axis_size("lat") - 1
    banded, distant = extend(fields)
    merged = banded.at[0].set(jnp.where(north, distant[0], banded[0]))
    merged = merged.at[-1].set(jnp.where(south, distant[1], merged[-1]))
    patches = jnp.concatenate(
        [
            merged[tap_row : tap_row + height, tap_col : tap_col + breadth].reshape(-1, channels)
            for tap_row in range(3)
            for tap_col in range(3)
        ],
        1,
    )
    conv_out = jnp.dot(
        patches, kernel.reshape(9 * channels, channels), preferred_element_type=jnp.float32
    )
    count = height * breadth * lax.axis_size("lat") * lax.axis_size("lon") * (channels // G)
    local_stats = jnp.concatenate(
        [jnp.sum(conv_out, 0).reshape(G, -1).sum(1), jnp.sum(conv_out * conv_out, 0).reshape(G, -1).sum(1)]
    )
    stats = butterfly_sum(local_stats)
    mean = stats[:G] / count
    var = stats[G:] / count - mean * mean
    rstd = lax.rsqrt(var + 1e-05)
    mean_ch = jnp.repeat(mean, channels // G)
    rstd_ch = jnp.repeat(rstd, channels // G)
    ghat = (conv_out - mean_ch) * rstd_ch
    pre = ghat * norm_gain + norm_shift
    sigma = jax.nn.sigmoid(pre)
    block_out = (
        (fields.reshape(-1, channels).astype(jnp.float32) + pre * sigma)
        .astype(jnp.bfloat16)
        .reshape(height, breadth, channels)
    )
    upstream = cotangent.astype(jnp.float32).reshape(-1, channels)
    dpre = upstream * (sigma * (1.0 + pre * (1.0 - sigma)))
    grad_sums = butterfly_sum(jnp.concatenate([jnp.sum(dpre * ghat, 0), jnp.sum(dpre, 0)]))
    grad_gain, grad_shift = grad_sums[:channels], grad_sums[channels:]
    mean_a = (norm_gain * grad_shift).reshape(G, -1).sum(1) / count
    mean_b = (norm_gain * grad_gain).reshape(G, -1).sum(1) / count
    dconv = (
        (
            dpre * norm_gain
            - jnp.repeat(mean_a, channels // G)
            - ghat * jnp.repeat(mean_b, channels // G)
        )
        * rstd_ch
    ).astype(jnp.bfloat16)
    grad_banded, grad_distant = extend(dconv.reshape(height, breadth, channels))
    grad_patches = jnp.concatenate(
        [
            grad_banded[
                2 - tap_row : 2 - tap_row + height, 2 - tap_col : 2 - tap_col + breadth
            ].reshape(-1, channels)
            for tap_row in range(3)
            for tap_col in range(3)
        ],
        1,
    )
    flipped = jnp.concatenate(
        [kernel[tap_row, tap_col].T for tap_row in range(3) for tap_col in range(3)], 0
    )
    back = jnp.dot(grad_patches, flipped, preferred_element_type=jnp.float32).reshape(
        height, breadth, channels
    )
    upper_term = jnp.zeros((breadth, channels), jnp.float32)
    lower_term = jnp.zeros((breadth, channels), jnp.float32)
    for tap_col in range(3):
        upper_term = upper_term + jnp.dot(
            grad_distant[0, 2 - tap_col : 2 - tap_col + breadth],
            kernel[0, tap_col].T,
            preferred_element_type=jnp.float32,
        )
        lower_term = lower_term + jnp.dot(
            grad_distant[1, 2 - tap_col : 2 - tap_col + breadth],
            kernel[2, tap_col].T,
            preferred_element_type=jnp.float32,
        )
    back = back.at[0].add(jnp.where(north, upper_term, 0.0))
    back = back.at[-1].add(jnp.where(south, lower_term, 0.0))
    grad_fields = (upstream.reshape(height, breadth, channels) + back).astype(jnp.bfloat16)
    lat_n, lon_n = lax.axis_size("lat"), lax.axis_size("lon")
    blocks = jnp.einsum(
        "njr,nio->ijro",
        patches.reshape(-1, lon_n, 9 * channels // lon_n),
        dconv.reshape(-1, lat_n, channels // lat_n),
        preferred_element_type=jnp.float32,
    )
    grad_kernel = halving_sum(blocks)
    return (block_out, grad_fields, grad_kernel, grad_gain, grad_shift)


def solution(mesh):
    in_specs = (P("lat", "lon", None), P(), P(), P(), P("lat", "lon", None))
    out_specs = (P("lat", "lon", None), P("lat", "lon", None), P("lon", "lat"), P(), P())
    return jax.shard_map(local, mesh=mesh, in_specs=in_specs, out_specs=out_specs, check_vma=False)
```

```python
import jax
import jax.numpy as jnp
from jax import lax
from jax.sharding import PartitionSpec as P

G = 32


def with_halo(shard, sides, width, wrap):
    for axis, dim in sides:
        peers, length = (lax.axis_size(axis), shard.shape[dim])
        up = [(i, (i + 1) % peers) for i in range(peers if wrap else peers - 1)]
        down = [(j, i) for i, j in up]
        last = lax.slice_in_dim(shard, length - width, length, axis=dim)
        initial = lax.slice_in_dim(shard, 0, width, axis=dim)
        before = lax.ppermute(last, axis, up)
        after = lax.ppermute(initial, axis, down)
        shard = jnp.concatenate([before, shard, after], axis=dim)
    return shard


def passed_along(block, axis, distance):
    devices = range(lax.axis_size(axis))
    route = [((i - distance) % len(devices), i) for i in devices]
    return lax.ppermute(block, axis, route)


def extend(field):
    halfway = lax.axis_size("lon") // 2
    widened = with_halo(field, (("lon", 1),), 1, True)
    banded = with_halo(widened, (("lat", 0),), 1, False)
    distant = passed_along(jnp.stack([widened[0], widened[-1]]), "lon", halfway)
    return (banded, distant)


def exchange(block, axis, bit):
    peers = lax.axis_size(axis)
    return lax.ppermute(block, axis, [(i, i ^ (1 << bit)) for i in range(peers)])


def butterfly_order():
    lat_bits = (lax.axis_size("lat") - 1).bit_length()
    lon_bits = (lax.axis_size("lon") - 1).bit_length()
    order = [("lat", b) for b in range(lat_bits)] + [("lon", b) for b in range(lon_bits)]
    return order


def butterfly_sum(value):
    for axis, bit in butterfly_order():
        value = value + exchange(value, axis, bit)
    return value


def halving_sum(term):
    lon_n = term.shape[0]
    lon_bits = (lon_n - 1).bit_length()
    lat_bits = (lax.axis_size("lat") - 1).bit_length()
    split = term.reshape((2,) * lon_bits + term.shape[1:])
    dims = {b: lon_bits - 1 - b for b in range(lon_bits)}

    def row_round(split, bit, dims):
        dim = dims[bit]
        mine = (lax.axis_index("lon") >> bit) & 1
        keep = lax.dynamic_index_in_dim(split, mine, dim, keepdims=False)
        send = lax.dynamic_index_in_dim(split, 1 - mine, dim, keepdims=False)
        dims = {k: (d - 1 if d > dim else d) for k, d in dims.items() if k != bit}
        return keep + exchange(send, "lon", bit), dims

    def col_round(split, bit):
        half = split.shape[-1] // 2
        mine = (lax.axis_index("lat") >> bit) & 1
        keep = lax.dynamic_slice_in_dim(split, mine * half, half, axis=split.ndim - 1)
        send = lax.dynamic_slice_in_dim(split, (1 - mine) * half, half, axis=split.ndim - 1)
        return keep + exchange(send, "lat", bit)

    split = col_round(split, 0)
    row_order = [0, 4, 1, 5, 2, 3] if lon_bits == 6 else list(range(lon_bits))
    for bit in row_order:
        split, dims = row_round(split, bit, dims)
    for bit in range(1, lat_bits):
        split = col_round(split, bit)
    return split


def local(fields, kernel, norm_gain, norm_shift, cotangent):
    height, breadth, channels = fields.shape
    north = lax.axis_index("lat") == 0
    south = lax.axis_index("lat") == lax.axis_size("lat") - 1
    banded, distant = extend(fields)
    merged = banded.at[0].set(jnp.where(north, distant[0], banded[0]))
    merged = merged.at[-1].set(jnp.where(south, distant[1], merged[-1]))
    patches = jnp.concatenate(
        [
            merged[tap_row : tap_row + height, tap_col : tap_col + breadth].reshape(-1, channels)
            for tap_row in range(3)
            for tap_col in range(3)
        ],
        1,
    )
    conv_out = jnp.dot(
        patches, kernel.reshape(9 * channels, channels), preferred_element_type=jnp.float32
    )
    count = height * breadth * lax.axis_size("lat") * lax.axis_size("lon") * (channels // G)
    local_stats = jnp.concatenate(
        [jnp.sum(conv_out, 0).reshape(G, -1).sum(1), jnp.sum(conv_out * conv_out, 0).reshape(G, -1).sum(1)]
    )
    stats = butterfly_sum(local_stats)
    mean = stats[:G] / count
    var = stats[G:] / count - mean * mean
    rstd = lax.rsqrt(var + 1e-05)
    mean_ch = jnp.repeat(mean, channels // G)
    rstd_ch = jnp.repeat(rstd, channels // G)
    ghat = (conv_out - mean_ch) * rstd_ch
    pre = ghat * norm_gain + norm_shift
    sigma = jax.nn.sigmoid(pre)
    block_out = (
        (fields.reshape(-1, channels).astype(jnp.float32) + pre * sigma)
        .astype(jnp.bfloat16)
        .reshape(height, breadth, channels)
    )
    upstream = cotangent.astype(jnp.float32).reshape(-1, channels)
    dpre = upstream * (sigma * (1.0 + pre * (1.0 - sigma)))
    grad_sums = butterfly_sum(jnp.concatenate([jnp.sum(dpre * ghat, 0), jnp.sum(dpre, 0)]))
    grad_gain, grad_shift = grad_sums[:channels], grad_sums[channels:]
    mean_a = (norm_gain * grad_shift).reshape(G, -1).sum(1) / count
    mean_b = (norm_gain * grad_gain).reshape(G, -1).sum(1) / count
    dconv = (
        (
            dpre * norm_gain
            - jnp.repeat(mean_a, channels // G)
            - ghat * jnp.repeat(mean_b, channels // G)
        )
        * rstd_ch
    ).astype(jnp.bfloat16)
    grad_banded, grad_distant = extend(dconv.reshape(height, breadth, channels))
    grad_patches = jnp.concatenate(
        [
            grad_banded[
                2 - tap_row : 2 - tap_row + height, 2 - tap_col : 2 - tap_col + breadth
            ].reshape(-1, channels)
            for tap_row in range(3)
            for tap_col in range(3)
        ],
        1,
    )
    flipped = jnp.concatenate(
        [kernel[tap_row, tap_col].T for tap_row in range(3) for tap_col in range(3)], 0
    )
    back = jnp.dot(grad_patches, flipped, preferred_element_type=jnp.float32).reshape(
        height, breadth, channels
    )
    upper_term = jnp.zeros((breadth, channels), jnp.float32)
    lower_term = jnp.zeros((breadth, channels), jnp.float32)
    for tap_col in range(3):
        upper_term = upper_term + jnp.dot(
            grad_distant[0, 2 - tap_col : 2 - tap_col + breadth],
            kernel[0, tap_col].T,
            preferred_element_type=jnp.float32,
        )
        lower_term = lower_term + jnp.dot(
            grad_distant[1, 2 - tap_col : 2 - tap_col + breadth],
            kernel[2, tap_col].T,
            preferred_element_type=jnp.float32,
        )
    back = back.at[0].add(jnp.where(north, upper_term, 0.0))
    back = back.at[-1].add(jnp.where(south, lower_term, 0.0))
    grad_fields = (upstream.reshape(height, breadth, channels) + back).astype(jnp.bfloat16)
    lat_n, lon_n = lax.axis_size("lat"), lax.axis_size("lon")
    lat_bits = (lat_n - 1).bit_length()
    lat_major = dconv.reshape((-1,) + (2,) * lat_bits + (channels // lat_n,))
    lat_major = lat_major.transpose((0,) + tuple(range(lat_bits, 0, -1)) + (lat_bits + 1,))
    blocks = jnp.einsum(
        "njr,nc->jrc",
        patches.reshape(-1, lon_n, 9 * channels // lon_n),
        lat_major.reshape(-1, channels),
        preferred_element_type=jnp.float32,
    )
    grad_kernel = halving_sum(blocks)
    return (block_out, grad_fields, grad_kernel, grad_gain, grad_shift)


def solution(mesh):
    in_specs = (P("lat", "lon", None), P(), P(), P(), P("lat", "lon", None))
    out_specs = (P("lat", "lon", None), P("lat", "lon", None), P("lon", "lat"), P(), P())
    return jax.shard_map(local, mesh=mesh, in_specs=in_specs, out_specs=out_specs, check_vma=False)
```

```python
import jax
import jax.numpy as jnp
from jax import lax
from jax.sharding import PartitionSpec as P

G = 32


def with_halo(shard, sides, width, wrap):
    for axis, dim in sides:
        peers, length = (lax.axis_size(axis), shard.shape[dim])
        up = [(i, (i + 1) % peers) for i in range(peers if wrap else peers - 1)]
        down = [(j, i) for i, j in up]
        last = lax.slice_in_dim(shard, length - width, length, axis=dim)
        initial = lax.slice_in_dim(shard, 0, width, axis=dim)
        before = lax.ppermute(last, axis, up)
        after = lax.ppermute(initial, axis, down)
        shard = jnp.concatenate([before, shard, after], axis=dim)
    return shard


def passed_along(block, axis, distance):
    devices = range(lax.axis_size(axis))
    route = [((i - distance) % len(devices), i) for i in devices]
    return lax.ppermute(block, axis, route)


def extend(field):
    halfway = lax.axis_size("lon") // 2
    widened = with_halo(field, (("lon", 1),), 1, True)
    banded = with_halo(widened, (("lat", 0),), 1, False)
    distant = passed_along(jnp.stack([widened[0], widened[-1]]), "lon", halfway)
    return (banded, distant)


def exchange(block, axis, bit):
    peers = lax.axis_size(axis)
    return lax.ppermute(block, axis, [(i, i ^ (1 << bit)) for i in range(peers)])


def butterfly_order():
    lat_bits = (lax.axis_size("lat") - 1).bit_length()
    lon_bits = (lax.axis_size("lon") - 1).bit_length()
    order = [("lat", b) for b in range(lat_bits)] + [("lon", b) for b in range(lon_bits)]
    return order


def butterfly_sum(value):
    for axis, bit in butterfly_order():
        value = value + exchange(value, axis, bit)
    return value


def halving_sum(term):
    lon_n = term.shape[0]
    lon_bits = (lon_n - 1).bit_length()
    lat_bits = (lax.axis_size("lat") - 1).bit_length()
    split = term.reshape((2,) * lon_bits + term.shape[1:])
    dims = {b: lon_bits - 1 - b for b in range(lon_bits)}

    def row_round(split, bit, dims):
        dim = dims[bit]
        mine = (lax.axis_index("lon") >> bit) & 1
        keep = lax.dynamic_index_in_dim(split, mine, dim, keepdims=False)
        send = lax.dynamic_index_in_dim(split, 1 - mine, dim, keepdims=False)
        dims = {k: (d - 1 if d > dim else d) for k, d in dims.items() if k != bit}
        return keep + exchange(send, "lon", bit), dims

    def col_round(split, bit):
        half = split.shape[-1] // 2
        mine = (lax.axis_index("lat") >> bit) & 1
        keep = lax.dynamic_slice_in_dim(split, mine * half, half, axis=split.ndim - 1)
        send = lax.dynamic_slice_in_dim(split, (1 - mine) * half, half, axis=split.ndim - 1)
        return keep + exchange(send, "lat", bit)

    split = col_round(split, 0)
    row_order = [0, 4, 1, 5, 2, 3] if lon_bits == 6 else list(range(lon_bits))
    for bit in row_order:
        split, dims = row_round(split, bit, dims)
    for bit in range(1, lat_bits):
        split = col_round(split, bit)
    return split


def conv_valid(field, weights):
    return lax.conv_general_dilated(
        field[None],
        weights,
        (1, 1),
        "VALID",
        dimension_numbers=("NHWC", "HWIO", "NHWC"),
        preferred_element_type=jnp.float32,
    )[0]


def local(fields, kernel, norm_gain, norm_shift, cotangent):
    height, breadth, channels = fields.shape
    north = lax.axis_index("lat") == 0
    south = lax.axis_index("lat") == lax.axis_size("lat") - 1
    banded, distant = extend(fields)
    merged = banded.at[0].set(jnp.where(north, distant[0], banded[0]))
    merged = merged.at[-1].set(jnp.where(south, distant[1], merged[-1]))
    conv_out = conv_valid(merged, kernel).reshape(-1, channels)
    count = height * breadth * lax.axis_size("lat") * lax.axis_size("lon") * (channels // G)
    local_stats = jnp.concatenate(
        [jnp.sum(conv_out, 0).reshape(G, -1).sum(1), jnp.sum(conv_out * conv_out, 0).reshape(G, -1).sum(1)]
    )
    stats = butterfly_sum(local_stats)
    mean = stats[:G] / count
    var = stats[G:] / count - mean * mean
    rstd = lax.rsqrt(var + 1e-05)
    mean_ch = jnp.repeat(mean, channels // G)
    rstd_ch = jnp.repeat(rstd, channels // G)
    ghat = (conv_out - mean_ch) * rstd_ch
    pre = ghat * norm_gain + norm_shift
    sigma = jax.nn.sigmoid(pre)
    block_out = (
        (fields.reshape(-1, channels).astype(jnp.float32) + pre * sigma)
        .astype(jnp.bfloat16)
        .reshape(height, breadth, channels)
    )
    upstream = cotangent.astype(jnp.float32).reshape(-1, channels)
    dpre = upstream * (sigma * (1.0 + pre * (1.0 - sigma)))
    grad_sums = butterfly_sum(jnp.concatenate([jnp.sum(dpre * ghat, 0), jnp.sum(dpre, 0)]))
    grad_gain, grad_shift = grad_sums[:channels], grad_sums[channels:]
    mean_a = (norm_gain * grad_shift).reshape(G, -1).sum(1) / count
    mean_b = (norm_gain * grad_gain).reshape(G, -1).sum(1) / count
    dconv = (
        (
            dpre * norm_gain
            - jnp.repeat(mean_a, channels // G)
            - ghat * jnp.repeat(mean_b, channels // G)
        )
        * rstd_ch
    ).astype(jnp.bfloat16)
    grad_banded, grad_distant = extend(dconv.reshape(height, breadth, channels))
    flipped = jnp.swapaxes(kernel[::-1, ::-1], 2, 3)
    back = conv_valid(grad_banded, flipped)
    upper_term = jnp.zeros((breadth, channels), jnp.float32)
    lower_term = jnp.zeros((breadth, channels), jnp.float32)
    for tap_col in range(3):
        upper_term = upper_term + jnp.dot(
            grad_distant[0, 2 - tap_col : 2 - tap_col + breadth],
            kernel[0, tap_col].T,
            preferred_element_type=jnp.float32,
        )
        lower_term = lower_term + jnp.dot(
            grad_distant[1, 2 - tap_col : 2 - tap_col + breadth],
            kernel[2, tap_col].T,
            preferred_element_type=jnp.float32,
        )
    back = back.at[0].add(jnp.where(north, upper_term, 0.0))
    back = back.at[-1].add(jnp.where(south, lower_term, 0.0))
    grad_fields = (upstream.reshape(height, breadth, channels) + back).astype(jnp.bfloat16)
    lat_n, lon_n = lax.axis_size("lat"), lax.axis_size("lon")
    lat_bits = (lat_n - 1).bit_length()
    lat_major = dconv.reshape((-1,) + (2,) * lat_bits + (channels // lat_n,))
    lat_major = lat_major.transpose((0,) + tuple(range(lat_bits, 0, -1)) + (lat_bits + 1,))
    term = lax.conv_general_dilated(
        merged[None],
        lat_major.reshape(height, breadth, 1, channels),
        (1, 1),
        "VALID",
        dimension_numbers=("CHWN", "HWIO", "HWNC"),
        preferred_element_type=jnp.float32,
    )
    blocks = term.reshape(lon_n, 9 * channels // lon_n, channels)
    grad_kernel = halving_sum(blocks)
    return (block_out, grad_fields, grad_kernel, grad_gain, grad_shift)


def solution(mesh):
    in_specs = (P("lat", "lon", None), P(), P(), P(), P("lat", "lon", None))
    out_specs = (P("lat", "lon", None), P("lat", "lon", None), P("lon", "lat"), P(), P())
    return jax.shard_map(local, mesh=mesh, in_specs=in_specs, out_specs=out_specs, check_vma=False)
```

```python
import jax
import jax.numpy as jnp
from jax import lax
from jax.sharding import PartitionSpec as P

G = 32


def with_halo(shard, sides, width, wrap):
    for axis, dim in sides:
        peers, length = (lax.axis_size(axis), shard.shape[dim])
        up = [(i, (i + 1) % peers) for i in range(peers if wrap else peers - 1)]
        down = [(j, i) for i, j in up]
        last = lax.slice_in_dim(shard, length - width, length, axis=dim)
        initial = lax.slice_in_dim(shard, 0, width, axis=dim)
        before = lax.ppermute(last, axis, up)
        after = lax.ppermute(initial, axis, down)
        shard = jnp.concatenate([before, shard, after], axis=dim)
    return shard


def passed_along(block, axis, distance):
    devices = range(lax.axis_size(axis))
    route = [((i - distance) % len(devices), i) for i in devices]
    return lax.ppermute(block, axis, route)


def extend(field):
    halfway = lax.axis_size("lon") // 2
    widened = with_halo(field, (("lon", 1),), 1, True)
    banded = with_halo(widened, (("lat", 0),), 1, False)
    distant = passed_along(jnp.stack([widened[0], widened[-1]]), "lon", halfway)
    return (banded, distant)


def exchange(block, axis, bit):
    peers = lax.axis_size(axis)
    return lax.ppermute(block, axis, [(i, i ^ (1 << bit)) for i in range(peers)])


def butterfly_order():
    lat_bits = (lax.axis_size("lat") - 1).bit_length()
    lon_bits = (lax.axis_size("lon") - 1).bit_length()
    order = [("lat", b) for b in range(lat_bits)] + [("lon", b) for b in range(lon_bits)]
    return order


def butterfly_sum(value):
    for axis, bit in butterfly_order():
        value = value + exchange(value, axis, bit)
    return value


def lon_halving_sum(rows):
    for bit in reversed(range((lax.axis_size("lon") - 1).bit_length())):
        half = rows.shape[1] // 2
        mine = (lax.axis_index("lon") >> bit) & 1
        keep = lax.dynamic_slice_in_dim(rows, mine * half, half, axis=1)
        send = lax.dynamic_slice_in_dim(rows, (1 - mine) * half, half, axis=1)
        rows = keep + exchange(send, "lon", bit)
    return rows


def conv_valid(field, weights):
    return lax.conv_general_dilated(
        field[None],
        weights,
        (1, 1),
        "VALID",
        dimension_numbers=("NHWC", "HWIO", "NHWC"),
        preferred_element_type=jnp.float32,
    )[0]


def local(fields, kernel, norm_gain, norm_shift, cotangent):
    height, breadth, channels = fields.shape
    north = lax.axis_index("lat") == 0
    south = lax.axis_index("lat") == lax.axis_size("lat") - 1
    banded, distant = extend(fields)
    merged = banded.at[0].set(jnp.where(north, distant[0], banded[0]))
    merged = merged.at[-1].set(jnp.where(south, distant[1], merged[-1]))
    conv_out = conv_valid(merged, kernel).reshape(-1, channels)
    count = height * breadth * lax.axis_size("lat") * lax.axis_size("lon") * (channels // G)
    local_stats = jnp.concatenate(
        [jnp.sum(conv_out, 0).reshape(G, -1).sum(1), jnp.sum(conv_out * conv_out, 0).reshape(G, -1).sum(1)]
    )
    stats = butterfly_sum(local_stats)
    mean = stats[:G] / count
    var = stats[G:] / count - mean * mean
    rstd = lax.rsqrt(var + 1e-05)
    mean_ch = jnp.repeat(mean, channels // G)
    rstd_ch = jnp.repeat(rstd, channels // G)
    ghat = (conv_out - mean_ch) * rstd_ch
    pre = ghat * norm_gain + norm_shift
    sigma = jax.nn.sigmoid(pre)
    block_out = (
        (fields.reshape(-1, channels).astype(jnp.float32) + pre * sigma)
        .astype(jnp.bfloat16)
        .reshape(height, breadth, channels)
    )
    upstream = cotangent.astype(jnp.float32).reshape(-1, channels)
    dpre = upstream * (sigma * (1.0 + pre * (1.0 - sigma)))
    pair_banded, pair_distant = extend(
        jnp.concatenate([dpre, ghat], 1).reshape(height, breadth, 2 * channels)
    )
    grad_sums = butterfly_sum(jnp.concatenate([jnp.sum(dpre * ghat, 0), jnp.sum(dpre, 0)]))
    grad_gain, grad_shift = grad_sums[:channels], grad_sums[channels:]
    mean_a = (norm_gain * grad_shift).reshape(G, -1).sum(1) / count
    mean_b = (norm_gain * grad_gain).reshape(G, -1).sum(1) / count

    def normalized_grad(pair):
        return (
            (
                pair[..., :channels] * norm_gain
                - jnp.repeat(mean_a, channels // G)
                - pair[..., channels:] * jnp.repeat(mean_b, channels // G)
            )
            * rstd_ch
        ).astype(jnp.bfloat16)

    grad_banded = normalized_grad(pair_banded)
    grad_distant = normalized_grad(pair_distant)
    dconv = grad_banded[1:-1, 1:-1]
    flipped = jnp.swapaxes(kernel[::-1, ::-1], 2, 3)
    back = conv_valid(grad_banded, flipped)
    upper_term = jnp.zeros((breadth, channels), jnp.float32)
    lower_term = jnp.zeros((breadth, channels), jnp.float32)
    for tap_col in range(3):
        upper_term = upper_term + jnp.dot(
            grad_distant[0, 2 - tap_col : 2 - tap_col + breadth],
            kernel[0, tap_col].T,
            preferred_element_type=jnp.float32,
        )
        lower_term = lower_term + jnp.dot(
            grad_distant[1, 2 - tap_col : 2 - tap_col + breadth],
            kernel[2, tap_col].T,
            preferred_element_type=jnp.float32,
        )
    back = back.at[0].add(jnp.where(north, upper_term, 0.0))
    back = back.at[-1].add(jnp.where(south, lower_term, 0.0))
    grad_fields = (upstream.reshape(height, breadth, channels) + back).astype(jnp.bfloat16)
    term = lax.conv_general_dilated(
        merged[None],
        dconv.reshape(height, breadth, 1, channels),
        (1, 1),
        "VALID",
        dimension_numbers=("CHWN", "HWIO", "CHWN"),
        preferred_element_type=jnp.float32,
    ).reshape(channels, 9 * channels)
    owned_cols = lax.psum_scatter(term, "lat", scatter_dimension=0, tiled=True)
    grad_kernel = lon_halving_sum(owned_cols).T
    return (block_out, grad_fields, grad_kernel, grad_gain, grad_shift)


def solution(mesh):
    in_specs = (P("lat", "lon", None), P(), P(), P(), P("lat", "lon", None))
    out_specs = (P("lat", "lon", None), P("lat", "lon", None), P("lon", "lat"), P(), P())
    return jax.shard_map(local, mesh=mesh, in_specs=in_specs, out_specs=out_specs, check_vma=False)
```

```python
import jax
import jax.numpy as jnp
from jax import lax
from jax.sharding import PartitionSpec as P

G = 32


def with_halo(shard, sides, width, wrap):
    for axis, dim in sides:
        peers, length = (lax.axis_size(axis), shard.shape[dim])
        up = [(i, (i + 1) % peers) for i in range(peers if wrap else peers - 1)]
        down = [(j, i) for i, j in up]
        last = lax.slice_in_dim(shard, length - width, length, axis=dim)
        initial = lax.slice_in_dim(shard, 0, width, axis=dim)
        before = lax.ppermute(last, axis, up)
        after = lax.ppermute(initial, axis, down)
        shard = jnp.concatenate([before, shard, after], axis=dim)
    return shard


def passed_along(block, axis, distance):
    devices = range(lax.axis_size(axis))
    route = [((i - distance) % len(devices), i) for i in devices]
    return lax.ppermute(block, axis, route)


def extend(field):
    halfway = lax.axis_size("lon") // 2
    widened = with_halo(field, (("lon", 1),), 1, True)
    banded = with_halo(widened, (("lat", 0),), 1, False)
    distant = passed_along(jnp.stack([widened[0], widened[-1]]), "lon", halfway)
    return (banded, distant)


def exchange(block, axis, bit):
    peers = lax.axis_size(axis)
    return lax.ppermute(block, axis, [(i, i ^ (1 << bit)) for i in range(peers)])


def butterfly_order():
    lat_bits = (lax.axis_size("lat") - 1).bit_length()
    lon_bits = (lax.axis_size("lon") - 1).bit_length()
    order = [("lat", b) for b in range(lat_bits)] + [("lon", b) for b in range(lon_bits)]
    return order


def butterfly_sum(value):
    for axis, bit in butterfly_order():
        value = value + exchange(value, axis, bit)
    return value


def lon_halving_sum(rows):
    for bit in reversed(range((lax.axis_size("lon") - 1).bit_length())):
        half = rows.shape[1] // 2
        mine = (lax.axis_index("lon") >> bit) & 1
        keep = lax.dynamic_slice_in_dim(rows, mine * half, half, axis=1)
        send = lax.dynamic_slice_in_dim(rows, (1 - mine) * half, half, axis=1)
        rows = keep + exchange(send, "lon", bit)
    return rows


def conv_valid(field, weights):
    return lax.conv_general_dilated(
        field[None],
        weights,
        (1, 1),
        "VALID",
        dimension_numbers=("NHWC", "HWIO", "NHWC"),
        preferred_element_type=jnp.float32,
    )[0]


def local(fields, kernel, norm_gain, norm_shift, cotangent):
    height, breadth, channels = fields.shape
    north = lax.axis_index("lat") == 0
    south = lax.axis_index("lat") == lax.axis_size("lat") - 1
    banded, distant = extend(fields)
    merged = banded.at[0].set(jnp.where(north, distant[0], banded[0]))
    merged = merged.at[-1].set(jnp.where(south, distant[1], merged[-1]))
    conv_out = conv_valid(merged, kernel).reshape(-1, channels)
    count = height * breadth * lax.axis_size("lat") * lax.axis_size("lon") * (channels // G)
    local_stats = jnp.concatenate(
        [jnp.sum(conv_out, 0).reshape(G, -1).sum(1), jnp.sum(conv_out * conv_out, 0).reshape(G, -1).sum(1)]
    )
    stats = butterfly_sum(local_stats)
    mean = stats[:G] / count
    var = stats[G:] / count - mean * mean
    rstd = lax.rsqrt(var + 1e-05)
    mean_ch = jnp.repeat(mean, channels // G)
    rstd_ch = jnp.repeat(rstd, channels // G)
    ghat = (conv_out - mean_ch) * rstd_ch
    pre = ghat * norm_gain + norm_shift
    sigma = jax.nn.sigmoid(pre)
    block_out = (
        (fields.reshape(-1, channels).astype(jnp.float32) + pre * sigma)
        .astype(jnp.bfloat16)
        .reshape(height, breadth, channels)
    )
    upstream = cotangent.astype(jnp.float32).reshape(-1, channels)
    dpre = upstream * (sigma * (1.0 + pre * (1.0 - sigma)))
    grad_sums = butterfly_sum(jnp.concatenate([jnp.sum(dpre * ghat, 0), jnp.sum(dpre, 0)]))
    grad_gain, grad_shift = grad_sums[:channels], grad_sums[channels:]
    mean_a = (norm_gain * grad_shift).reshape(G, -1).sum(1) / count
    mean_b = (norm_gain * grad_gain).reshape(G, -1).sum(1) / count
    dconv = (
        (
            dpre * norm_gain
            - jnp.repeat(mean_a, channels // G)
            - ghat * jnp.repeat(mean_b, channels // G)
        )
        * rstd_ch
    ).astype(jnp.bfloat16)
    dconv = dconv.reshape(height, breadth, channels)
    term = lax.conv_general_dilated(
        merged[None],
        dconv.reshape(height, breadth, 1, channels),
        (1, 1),
        "VALID",
        dimension_numbers=("CHWN", "HWIO", "CHWN"),
        preferred_element_type=jnp.float32,
    ).reshape(channels, 9 * channels)
    owned_cols = lax.psum_scatter(term, "lat", scatter_dimension=0, tiled=True)
    grad_banded, grad_distant = extend(dconv)
    flipped = jnp.swapaxes(kernel[::-1, ::-1], 2, 3)
    back = conv_valid(grad_banded, flipped)
    upper_term = jnp.zeros((breadth, channels), jnp.float32)
    lower_term = jnp.zeros((breadth, channels), jnp.float32)
    for tap_col in range(3):
        upper_term = upper_term + jnp.dot(
            grad_distant[0, 2 - tap_col : 2 - tap_col + breadth],
            kernel[0, tap_col].T,
            preferred_element_type=jnp.float32,
        )
        lower_term = lower_term + jnp.dot(
            grad_distant[1, 2 - tap_col : 2 - tap_col + breadth],
            kernel[2, tap_col].T,
            preferred_element_type=jnp.float32,
        )
    back = back.at[0].add(jnp.where(north, upper_term, 0.0))
    back = back.at[-1].add(jnp.where(south, lower_term, 0.0))
    grad_fields = (upstream.reshape(height, breadth, channels) + back).astype(jnp.bfloat16)
    grad_kernel = lon_halving_sum(owned_cols).T
    return (block_out, grad_fields, grad_kernel, grad_gain, grad_shift)


def solution(mesh):
    in_specs = (P("lat", "lon", None), P(), P(), P(), P("lat", "lon", None))
    out_specs = (P("lat", "lon", None), P("lat", "lon", None), P("lon", "lat"), P(), P())
    return jax.shard_map(local, mesh=mesh, in_specs=in_specs, out_specs=out_specs, check_vma=False)
```

```python
import jax
import jax.numpy as jnp
from jax import lax
from jax.sharding import PartitionSpec as P

G = 32


def with_halo(shard, sides, width, wrap):
    for axis, dim in sides:
        peers, length = (lax.axis_size(axis), shard.shape[dim])
        up = [(i, (i + 1) % peers) for i in range(peers if wrap else peers - 1)]
        down = [(j, i) for i, j in up]
        last = lax.slice_in_dim(shard, length - width, length, axis=dim)
        initial = lax.slice_in_dim(shard, 0, width, axis=dim)
        if width == 1:
            before = jnp.expand_dims(lax.ppermute(jnp.squeeze(last, dim), axis, up), dim)
            after = jnp.expand_dims(lax.ppermute(jnp.squeeze(initial, dim), axis, down), dim)
        else:
            before = lax.ppermute(last, axis, up)
            after = lax.ppermute(initial, axis, down)
        shard = jnp.concatenate([before, shard, after], axis=dim)
    return shard


def passed_along(block, axis, distance):
    devices = range(lax.axis_size(axis))
    route = [((i - distance) % len(devices), i) for i in devices]
    return lax.ppermute(block, axis, route)


def extend(field):
    halfway = lax.axis_size("lon") // 2
    widened = with_halo(field, (("lon", 1),), 1, True)
    banded = with_halo(widened, (("lat", 0),), 1, False)
    distant = passed_along(jnp.stack([widened[0], widened[-1]]), "lon", halfway)
    return (banded, distant)


def exchange(block, axis, bit):
    peers = lax.axis_size(axis)
    return lax.ppermute(block, axis, [(i, i ^ (1 << bit)) for i in range(peers)])


def butterfly_order():
    lat_bits = (lax.axis_size("lat") - 1).bit_length()
    lon_bits = (lax.axis_size("lon") - 1).bit_length()
    order = [("lat", b) for b in range(lat_bits)] + [("lon", b) for b in range(lon_bits)]
    return order


def butterfly_sum(value):
    for axis, bit in butterfly_order():
        value = value + exchange(value, axis, bit)
    return value


def lon_halving_sum(rows):
    for bit in reversed(range((lax.axis_size("lon") - 1).bit_length())):
        half = rows.shape[1] // 2
        mine = (lax.axis_index("lon") >> bit) & 1
        keep = lax.dynamic_slice_in_dim(rows, mine * half, half, axis=1)
        send = lax.dynamic_slice_in_dim(rows, (1 - mine) * half, half, axis=1)
        rows = keep + exchange(send, "lon", bit)
    return rows


def conv_valid(field, weights):
    return lax.conv_general_dilated(
        field[None],
        weights,
        (1, 1),
        "VALID",
        dimension_numbers=("NHWC", "HWIO", "NHWC"),
        preferred_element_type=jnp.float32,
    )[0]


def local(fields, kernel, norm_gain, norm_shift, cotangent):
    height, breadth, channels = fields.shape
    north = lax.axis_index("lat") == 0
    south = lax.axis_index("lat") == lax.axis_size("lat") - 1
    banded, distant = extend(fields)
    merged = banded.at[0].set(jnp.where(north, distant[0], banded[0]))
    merged = merged.at[-1].set(jnp.where(south, distant[1], merged[-1]))
    conv_out = conv_valid(merged, kernel).reshape(-1, channels)
    count = height * breadth * lax.axis_size("lat") * lax.axis_size("lon") * (channels // G)
    local_stats = jnp.concatenate(
        [jnp.sum(conv_out, 0).reshape(G, -1).sum(1), jnp.sum(conv_out * conv_out, 0).reshape(G, -1).sum(1)]
    )
    stats = butterfly_sum(local_stats)
    mean = stats[:G] / count
    var = stats[G:] / count - mean * mean
    rstd = lax.rsqrt(var + 1e-05)
    mean_ch = jnp.repeat(mean, channels // G)
    rstd_ch = jnp.repeat(rstd, channels // G)
    ghat = (conv_out - mean_ch) * rstd_ch
    pre = ghat * norm_gain + norm_shift
    sigma = jax.nn.sigmoid(pre)
    block_out = (
        (fields.reshape(-1, channels).astype(jnp.float32) + pre * sigma)
        .astype(jnp.bfloat16)
        .reshape(height, breadth, channels)
    )
    upstream = cotangent.astype(jnp.float32).reshape(-1, channels)
    dpre = upstream * (sigma * (1.0 + pre * (1.0 - sigma)))
    grad_sums = butterfly_sum(jnp.concatenate([jnp.sum(dpre * ghat, 0), jnp.sum(dpre, 0)]))
    grad_gain, grad_shift = grad_sums[:channels], grad_sums[channels:]
    mean_a = (norm_gain * grad_shift).reshape(G, -1).sum(1) / count
    mean_b = (norm_gain * grad_gain).reshape(G, -1).sum(1) / count
    dconv = (
        (
            dpre * norm_gain
            - jnp.repeat(mean_a, channels // G)
            - ghat * jnp.repeat(mean_b, channels // G)
        )
        * rstd_ch
    ).astype(jnp.bfloat16)
    dconv = dconv.reshape(height, breadth, channels)
    term = lax.conv_general_dilated(
        merged[None],
        dconv.reshape(height, breadth, 1, channels),
        (1, 1),
        "VALID",
        dimension_numbers=("CHWN", "HWIO", "CHWN"),
        preferred_element_type=jnp.float32,
    ).reshape(channels, 9 * channels)
    owned_cols = lax.psum_scatter(term, "lat", scatter_dimension=0, tiled=True)
    grad_banded, grad_distant = extend(dconv)
    flipped = jnp.swapaxes(kernel[::-1, ::-1], 2, 3)
    back = conv_valid(grad_banded, flipped)
    upper_term = jnp.zeros((breadth, channels), jnp.float32)
    lower_term = jnp.zeros((breadth, channels), jnp.float32)
    for tap_col in range(3):
        upper_term = upper_term + jnp.dot(
            grad_distant[0, 2 - tap_col : 2 - tap_col + breadth],
            kernel[0, tap_col].T,
            preferred_element_type=jnp.float32,
        )
        lower_term = lower_term + jnp.dot(
            grad_distant[1, 2 - tap_col : 2 - tap_col + breadth],
            kernel[2, tap_col].T,
            preferred_element_type=jnp.float32,
        )
    back = back.at[0].add(jnp.where(north, upper_term, 0.0))
    back = back.at[-1].add(jnp.where(south, lower_term, 0.0))
    grad_fields = (upstream.reshape(height, breadth, channels) + back).astype(jnp.bfloat16)
    grad_kernel = lon_halving_sum(owned_cols).T
    return (block_out, grad_fields, grad_kernel, grad_gain, grad_shift)


def solution(mesh):
    in_specs = (P("lat", "lon", None), P(), P(), P(), P("lat", "lon", None))
    out_specs = (P("lat", "lon", None), P("lat", "lon", None), P("lon", "lat"), P(), P())
    return jax.shard_map(local, mesh=mesh, in_specs=in_specs, out_specs=out_specs, check_vma=False)
```

```python
import jax
import jax.numpy as jnp
from jax import lax
from jax.sharding import PartitionSpec as P

G = 32


def with_halo(shard, sides, width, wrap):
    for axis, dim in sides:
        peers, length = (lax.axis_size(axis), shard.shape[dim])
        up = [(i, (i + 1) % peers) for i in range(peers if wrap else peers - 1)]
        down = [(j, i) for i, j in up]
        last = lax.slice_in_dim(shard, length - width, length, axis=dim)
        initial = lax.slice_in_dim(shard, 0, width, axis=dim)
        if width == 1:
            before = jnp.expand_dims(lax.ppermute(jnp.squeeze(last, dim), axis, up), dim)
            after = jnp.expand_dims(lax.ppermute(jnp.squeeze(initial, dim), axis, down), dim)
        else:
            before = lax.ppermute(last, axis, up)
            after = lax.ppermute(initial, axis, down)
        shard = jnp.concatenate([before, shard, after], axis=dim)
    return shard


def passed_along(block, axis, distance):
    devices = range(lax.axis_size(axis))
    route = [((i - distance) % len(devices), i) for i in devices]
    return lax.ppermute(block, axis, route)


def extend(field):
    halfway = lax.axis_size("lon") // 2
    widened = with_halo(field, (("lon", 1),), 1, True)
    banded = with_halo(widened, (("lat", 0),), 1, False)
    distant = passed_along(jnp.stack([widened[0], widened[-1]]), "lon", halfway)
    return (banded, distant)


def exchange(block, axis, bit):
    peers = lax.axis_size(axis)
    return lax.ppermute(block, axis, [(i, i ^ (1 << bit)) for i in range(peers)])


def butterfly_order():
    lat_bits = (lax.axis_size("lat") - 1).bit_length()
    lon_bits = (lax.axis_size("lon") - 1).bit_length()
    order = [("lat", b) for b in range(lat_bits)] + [("lon", b) for b in range(lon_bits)]
    return order


def butterfly_sum(value):
    value = jnp.sum(lax.all_gather(value, "lat"), 0)
    for bit in range((lax.axis_size("lon") - 1).bit_length()):
        value = value + exchange(value, "lon", bit)
    return value


def lon_halving_sum(rows):
    for bit in reversed(range((lax.axis_size("lon") - 1).bit_length())):
        half = rows.shape[1] // 2
        mine = (lax.axis_index("lon") >> bit) & 1
        keep = lax.dynamic_slice_in_dim(rows, mine * half, half, axis=1)
        send = lax.dynamic_slice_in_dim(rows, (1 - mine) * half, half, axis=1)
        rows = keep + exchange(send, "lon", bit)
    return rows


def conv_valid(field, weights):
    return lax.conv_general_dilated(
        field[None],
        weights,
        (1, 1),
        "VALID",
        dimension_numbers=("NHWC", "HWIO", "NHWC"),
        preferred_element_type=jnp.float32,
    )[0]


def local(fields, kernel, norm_gain, norm_shift, cotangent):
    height, breadth, channels = fields.shape
    north = lax.axis_index("lat") == 0
    south = lax.axis_index("lat") == lax.axis_size("lat") - 1
    banded, distant = extend(fields)
    merged = banded.at[0].set(jnp.where(north, distant[0], banded[0]))
    merged = merged.at[-1].set(jnp.where(south, distant[1], merged[-1]))
    conv_out = conv_valid(merged, kernel).reshape(-1, channels)
    count = height * breadth * lax.axis_size("lat") * lax.axis_size("lon") * (channels // G)
    local_stats = jnp.concatenate(
        [jnp.sum(conv_out, 0).reshape(G, -1).sum(1), jnp.sum(conv_out * conv_out, 0).reshape(G, -1).sum(1)]
    )
    stats = butterfly_sum(local_stats)
    mean = stats[:G] / count
    var = stats[G:] / count - mean * mean
    rstd = lax.rsqrt(var + 1e-05)
    mean_ch = jnp.repeat(mean, channels // G)
    rstd_ch = jnp.repeat(rstd, channels // G)
    ghat = (conv_out - mean_ch) * rstd_ch
    pre = ghat * norm_gain + norm_shift
    sigma = jax.nn.sigmoid(pre)
    block_out = (
        (fields.reshape(-1, channels).astype(jnp.float32) + pre * sigma)
        .astype(jnp.bfloat16)
        .reshape(height, breadth, channels)
    )
    upstream = cotangent.astype(jnp.float32).reshape(-1, channels)
    dpre = upstream * (sigma * (1.0 + pre * (1.0 - sigma)))
    grad_sums = butterfly_sum(jnp.concatenate([jnp.sum(dpre * ghat, 0), jnp.sum(dpre, 0)]))
    grad_gain, grad_shift = grad_sums[:channels], grad_sums[channels:]
    mean_a = (norm_gain * grad_shift).reshape(G, -1).sum(1) / count
    mean_b = (norm_gain * grad_gain).reshape(G, -1).sum(1) / count
    dconv = (
        (
            dpre * norm_gain
            - jnp.repeat(mean_a, channels // G)
            - ghat * jnp.repeat(mean_b, channels // G)
        )
        * rstd_ch
    ).astype(jnp.bfloat16)
    dconv = dconv.reshape(height, breadth, channels)
    term = lax.conv_general_dilated(
        merged[None],
        dconv.reshape(height, breadth, 1, channels),
        (1, 1),
        "VALID",
        dimension_numbers=("CHWN", "HWIO", "CHWN"),
        preferred_element_type=jnp.float32,
    ).reshape(channels, 9 * channels)
    owned_cols = lax.psum_scatter(term, "lat", scatter_dimension=0, tiled=True)
    grad_banded, grad_distant = extend(dconv)
    flipped = jnp.swapaxes(kernel[::-1, ::-1], 2, 3)
    back = conv_valid(grad_banded, flipped)
    upper_term = jnp.zeros((breadth, channels), jnp.float32)
    lower_term = jnp.zeros((breadth, channels), jnp.float32)
    for tap_col in range(3):
        upper_term = upper_term + jnp.dot(
            grad_distant[0, 2 - tap_col : 2 - tap_col + breadth],
            kernel[0, tap_col].T,
            preferred_element_type=jnp.float32,
        )
        lower_term = lower_term + jnp.dot(
            grad_distant[1, 2 - tap_col : 2 - tap_col + breadth],
            kernel[2, tap_col].T,
            preferred_element_type=jnp.float32,
        )
    back = back.at[0].add(jnp.where(north, upper_term, 0.0))
    back = back.at[-1].add(jnp.where(south, lower_term, 0.0))
    grad_fields = (upstream.reshape(height, breadth, channels) + back).astype(jnp.bfloat16)
    grad_kernel = lon_halving_sum(owned_cols).T
    return (block_out, grad_fields, grad_kernel, grad_gain, grad_shift)


def solution(mesh):
    in_specs = (P("lat", "lon", None), P(), P(), P(), P("lat", "lon", None))
    out_specs = (P("lat", "lon", None), P("lat", "lon", None), P("lon", "lat"), P(), P())
    return jax.shard_map(local, mesh=mesh, in_specs=in_specs, out_specs=out_specs, check_vma=False)
```

```python
import jax
import jax.numpy as jnp
from jax import lax
from jax.sharding import PartitionSpec as P

G = 32


def with_halo(shard, sides, width, wrap):
    for axis, dim in sides:
        peers, length = (lax.axis_size(axis), shard.shape[dim])
        up = [(i, (i + 1) % peers) for i in range(peers if wrap else peers - 1)]
        down = [(j, i) for i, j in up]
        last = lax.slice_in_dim(shard, length - width, length, axis=dim)
        initial = lax.slice_in_dim(shard, 0, width, axis=dim)
        if width == 1:
            before = jnp.expand_dims(lax.ppermute(jnp.squeeze(last, dim), axis, up), dim)
            after = jnp.expand_dims(lax.ppermute(jnp.squeeze(initial, dim), axis, down), dim)
        else:
            before = lax.ppermute(last, axis, up)
            after = lax.ppermute(initial, axis, down)
        shard = jnp.concatenate([before, shard, after], axis=dim)
    return shard


def passed_along(block, axis, distance):
    devices = range(lax.axis_size(axis))
    route = [((i - distance) % len(devices), i) for i in devices]
    return lax.ppermute(block, axis, route)


def extend(field):
    halfway = lax.axis_size("lon") // 2
    widened = with_halo(field, (("lon", 1),), 1, True)
    banded = with_halo(widened, (("lat", 0),), 1, False)
    distant = passed_along(jnp.stack([widened[0], widened[-1]]), "lon", halfway)
    return (banded, distant)


def exchange(block, axis, bit):
    peers = lax.axis_size(axis)
    return lax.ppermute(block, axis, [(i, i ^ (1 << bit)) for i in range(peers)])


def butterfly_order():
    lat_bits = (lax.axis_size("lat") - 1).bit_length()
    lon_bits = (lax.axis_size("lon") - 1).bit_length()
    order = [("lat", b) for b in range(lat_bits)] + [("lon", b) for b in range(lon_bits)]
    return order


def butterfly_sum(value):
    value = jnp.sum(lax.all_gather(value, "lat"), 0)
    for bit in range((lax.axis_size("lon") - 1).bit_length()):
        value = value + exchange(value, "lon", bit)
    return value


def lon_halving_sum(rows, bits):
    for bit in reversed(range(bits)):
        half = rows.shape[1] // 2
        mine = (lax.axis_index("lon") >> bit) & 1
        keep = lax.dynamic_slice_in_dim(rows, mine * half, half, axis=1)
        send = lax.dynamic_slice_in_dim(rows, (1 - mine) * half, half, axis=1)
        rows = keep + exchange(send, "lon", bit)
    return rows


def conv_valid(field, weights):
    return lax.conv_general_dilated(
        field[None],
        weights,
        (1, 1),
        "VALID",
        dimension_numbers=("NHWC", "HWIO", "NHWC"),
        preferred_element_type=jnp.float32,
    )[0]


def local(fields, kernel, norm_gain, norm_shift, cotangent):
    height, breadth, channels = fields.shape
    north = lax.axis_index("lat") == 0
    south = lax.axis_index("lat") == lax.axis_size("lat") - 1
    banded, distant = extend(fields)
    merged = banded.at[0].set(jnp.where(north, distant[0], banded[0]))
    merged = merged.at[-1].set(jnp.where(south, distant[1], merged[-1]))
    conv_out = conv_valid(merged, kernel).reshape(-1, channels)
    count = height * breadth * lax.axis_size("lat") * lax.axis_size("lon") * (channels // G)
    local_stats = jnp.concatenate(
        [jnp.sum(conv_out, 0).reshape(G, -1).sum(1), jnp.sum(conv_out * conv_out, 0).reshape(G, -1).sum(1)]
    )
    stats = butterfly_sum(local_stats)
    mean = stats[:G] / count
    var = stats[G:] / count - mean * mean
    rstd = lax.rsqrt(var + 1e-05)
    mean_ch = jnp.repeat(mean, channels // G)
    rstd_ch = jnp.repeat(rstd, channels // G)
    ghat = (conv_out - mean_ch) * rstd_ch
    pre = ghat * norm_gain + norm_shift
    sigma = jax.nn.sigmoid(pre)
    block_out = (
        (fields.reshape(-1, channels).astype(jnp.float32) + pre * sigma)
        .astype(jnp.bfloat16)
        .reshape(height, breadth, channels)
    )
    upstream = cotangent.astype(jnp.float32).reshape(-1, channels)
    dpre = upstream * (sigma * (1.0 + pre * (1.0 - sigma)))
    grad_sums = butterfly_sum(jnp.concatenate([jnp.sum(dpre * ghat, 0), jnp.sum(dpre, 0)]))
    grad_gain, grad_shift = grad_sums[:channels], grad_sums[channels:]
    mean_a = (norm_gain * grad_shift).reshape(G, -1).sum(1) / count
    mean_b = (norm_gain * grad_gain).reshape(G, -1).sum(1) / count
    dconv = (
        (
            dpre * norm_gain
            - jnp.repeat(mean_a, channels // G)
            - ghat * jnp.repeat(mean_b, channels // G)
        )
        * rstd_ch
    ).astype(jnp.bfloat16)
    dconv = dconv.reshape(height, breadth, channels)
    term = lax.conv_general_dilated(
        merged[None],
        dconv.reshape(height, breadth, 1, channels),
        (1, 1),
        "VALID",
        dimension_numbers=("CHWN", "HWIO", "CHWN"),
        preferred_element_type=jnp.float32,
    ).reshape(channels, 9 * channels)
    top = (lax.axis_size("lon") - 1).bit_length() - 1
    half = term.shape[1] // 2
    mine = (lax.axis_index("lon") >> top) & 1
    sent = lax.psum_scatter(
        lax.dynamic_slice_in_dim(term, (1 - mine) * half, half, axis=1), "lat", scatter_dimension=0, tiled=True
    )
    kept = lax.psum_scatter(
        lax.dynamic_slice_in_dim(term, mine * half, half, axis=1), "lat", scatter_dimension=0, tiled=True
    )
    grad_banded, grad_distant = extend(dconv)
    flipped = jnp.swapaxes(kernel[::-1, ::-1], 2, 3)
    back = conv_valid(grad_banded, flipped)
    upper_term = jnp.zeros((breadth, channels), jnp.float32)
    lower_term = jnp.zeros((breadth, channels), jnp.float32)
    for tap_col in range(3):
        upper_term = upper_term + jnp.dot(
            grad_distant[0, 2 - tap_col : 2 - tap_col + breadth],
            kernel[0, tap_col].T,
            preferred_element_type=jnp.float32,
        )
        lower_term = lower_term + jnp.dot(
            grad_distant[1, 2 - tap_col : 2 - tap_col + breadth],
            kernel[2, tap_col].T,
            preferred_element_type=jnp.float32,
        )
    back = back.at[0].add(jnp.where(north, upper_term, 0.0))
    back = back.at[-1].add(jnp.where(south, lower_term, 0.0))
    grad_fields = (upstream.reshape(height, breadth, channels) + back).astype(jnp.bfloat16)
    grad_kernel = lon_halving_sum(kept + exchange(sent, "lon", top), top).T
    return (block_out, grad_fields, grad_kernel, grad_gain, grad_shift)


def solution(mesh):
    in_specs = (P("lat", "lon", None), P(), P(), P(), P("lat", "lon", None))
    out_specs = (P("lat", "lon", None), P("lat", "lon", None), P("lon", "lat"), P(), P())
    return jax.shard_map(local, mesh=mesh, in_specs=in_specs, out_specs=out_specs, check_vma=False)
```

```python
import jax
import jax.numpy as jnp
from jax import lax
from jax.sharding import PartitionSpec as P

G = 32


def with_halo(shard, sides, width, wrap):
    for axis, dim in sides:
        peers, length = (lax.axis_size(axis), shard.shape[dim])
        up = [(i, (i + 1) % peers) for i in range(peers if wrap else peers - 1)]
        down = [(j, i) for i, j in up]
        last = lax.slice_in_dim(shard, length - width, length, axis=dim)
        initial = lax.slice_in_dim(shard, 0, width, axis=dim)
        if width == 1:
            before = jnp.expand_dims(lax.ppermute(jnp.squeeze(last, dim), axis, up), dim)
            after = jnp.expand_dims(lax.ppermute(jnp.squeeze(initial, dim), axis, down), dim)
        else:
            before = lax.ppermute(last, axis, up)
            after = lax.ppermute(initial, axis, down)
        shard = jnp.concatenate([before, shard, after], axis=dim)
    return shard


def passed_along(block, axis, distance):
    devices = range(lax.axis_size(axis))
    route = [((i - distance) % len(devices), i) for i in devices]
    return lax.ppermute(block, axis, route)


def extend(field):
    halfway = lax.axis_size("lon") // 2
    widened = with_halo(field, (("lon", 1),), 1, True)
    banded = with_halo(widened, (("lat", 0),), 1, False)
    distant = passed_along(jnp.stack([widened[0], widened[-1]]), "lon", halfway)
    return (banded, distant)


def exchange(block, axis, bit):
    peers = lax.axis_size(axis)
    return lax.ppermute(block, axis, [(i, i ^ (1 << bit)) for i in range(peers)])


def butterfly_order():
    lat_bits = (lax.axis_size("lat") - 1).bit_length()
    lon_bits = (lax.axis_size("lon") - 1).bit_length()
    order = [("lat", b) for b in range(lat_bits)] + [("lon", b) for b in range(lon_bits)]
    return order


def butterfly_sum(value):
    value = jnp.sum(lax.all_gather(value, "lat"), 0)
    for bit in range((lax.axis_size("lon") - 1).bit_length()):
        value = value + exchange(value, "lon", bit)
    return value


def lon_halving_sum(rows):
    for bit in reversed(range((lax.axis_size("lon") - 1).bit_length())):
        half = rows.shape[1] // 2
        mine = (lax.axis_index("lon") >> bit) & 1
        keep = lax.dynamic_slice_in_dim(rows, mine * half, half, axis=1)
        send = lax.dynamic_slice_in_dim(rows, (1 - mine) * half, half, axis=1)
        rows = keep + exchange(send, "lon", bit)
    return rows


def conv_valid(field, weights):
    return lax.conv_general_dilated(
        field[None],
        weights,
        (1, 1),
        "VALID",
        dimension_numbers=("NHWC", "HWIO", "NHWC"),
        preferred_element_type=jnp.float32,
    )[0]


def local(fields, kernel, norm_gain, norm_shift, cotangent):
    height, breadth, channels = fields.shape
    north = lax.axis_index("lat") == 0
    south = lax.axis_index("lat") == lax.axis_size("lat") - 1
    banded, distant = extend(fields)
    merged = banded.at[0].set(jnp.where(north, distant[0], banded[0]))
    merged = merged.at[-1].set(jnp.where(south, distant[1], merged[-1]))
    conv_out = conv_valid(merged, kernel).reshape(-1, channels)
    count = height * breadth * lax.axis_size("lat") * lax.axis_size("lon") * (channels // G)
    local_stats = jnp.concatenate(
        [jnp.sum(conv_out, 0).reshape(G, -1).sum(1), jnp.sum(conv_out * conv_out, 0).reshape(G, -1).sum(1)]
    )
    stats = butterfly_sum(local_stats)
    mean = stats[:G] / count
    var = stats[G:] / count - mean * mean
    rstd = lax.rsqrt(var + 1e-05)
    mean_ch = jnp.repeat(mean, channels // G)
    rstd_ch = jnp.repeat(rstd, channels // G)
    ghat = (conv_out - mean_ch) * rstd_ch
    pre = ghat * norm_gain + norm_shift
    sigma = jax.nn.sigmoid(pre)
    block_out = (
        (fields.reshape(-1, channels).astype(jnp.float32) + pre * sigma)
        .astype(jnp.bfloat16)
        .reshape(height, breadth, channels)
    )
    upstream = cotangent.astype(jnp.float32).reshape(-1, channels)
    dpre = upstream * (sigma * (1.0 + pre * (1.0 - sigma)))
    grad_sums = butterfly_sum(jnp.concatenate([jnp.sum(dpre * ghat, 0), jnp.sum(dpre, 0)]))
    grad_gain, grad_shift = grad_sums[:channels], grad_sums[channels:]
    mean_a = (norm_gain * grad_shift).reshape(G, -1).sum(1) / count
    mean_b = (norm_gain * grad_gain).reshape(G, -1).sum(1) / count
    dconv = (
        (
            dpre * norm_gain
            - jnp.repeat(mean_a, channels // G)
            - ghat * jnp.repeat(mean_b, channels // G)
        )
        * rstd_ch
    ).astype(jnp.bfloat16)
    dconv = dconv.reshape(height, breadth, channels)
    term = lax.conv_general_dilated(
        merged[None],
        dconv.reshape(height, breadth, 1, channels),
        (1, 1),
        "VALID",
        dimension_numbers=("CHWN", "HWIO", "CHWN"),
        preferred_element_type=jnp.float32,
    )
    owned_cols = lax.psum_scatter(term, "lat", scatter_dimension=0, tiled=True)
    owned_cols = owned_cols.reshape(owned_cols.shape[0], 9 * channels)
    grad_banded, grad_distant = extend(dconv)
    flipped = jnp.swapaxes(kernel[::-1, ::-1], 2, 3)
    back = conv_valid(grad_banded, flipped)
    upper_term = jnp.zeros((breadth, channels), jnp.float32)
    lower_term = jnp.zeros((breadth, channels), jnp.float32)
    for tap_col in range(3):
        upper_term = upper_term + jnp.dot(
            grad_distant[0, 2 - tap_col : 2 - tap_col + breadth],
            kernel[0, tap_col].T,
            preferred_element_type=jnp.float32,
        )
        lower_term = lower_term + jnp.dot(
            grad_distant[1, 2 - tap_col : 2 - tap_col + breadth],
            kernel[2, tap_col].T,
            preferred_element_type=jnp.float32,
        )
    back = back.at[0].add(jnp.where(north, upper_term, 0.0))
    back = back.at[-1].add(jnp.where(south, lower_term, 0.0))
    grad_fields = (upstream.reshape(height, breadth, channels) + back).astype(jnp.bfloat16)
    grad_kernel = lon_halving_sum(owned_cols).T
    return (block_out, grad_fields, grad_kernel, grad_gain, grad_shift)


def solution(mesh):
    in_specs = (P("lat", "lon", None), P(), P(), P(), P("lat", "lon", None))
    out_specs = (P("lat", "lon", None), P("lat", "lon", None), P("lon", "lat"), P(), P())
    return jax.shard_map(local, mesh=mesh, in_specs=in_specs, out_specs=out_specs, check_vma=False)
```

```python
import jax
import jax.numpy as jnp
from jax import lax
from jax.sharding import PartitionSpec as P

G = 32


def with_halo(shard, sides, width, wrap):
    for axis, dim in sides:
        peers, length = (lax.axis_size(axis), shard.shape[dim])
        up = [(i, (i + 1) % peers) for i in range(peers if wrap else peers - 1)]
        down = [(j, i) for i, j in up]
        last = lax.slice_in_dim(shard, length - width, length, axis=dim)
        initial = lax.slice_in_dim(shard, 0, width, axis=dim)
        if width == 1:
            before = jnp.expand_dims(lax.ppermute(jnp.squeeze(last, dim), axis, up), dim)
            after = jnp.expand_dims(lax.ppermute(jnp.squeeze(initial, dim), axis, down), dim)
        else:
            before = lax.ppermute(last, axis, up)
            after = lax.ppermute(initial, axis, down)
        shard = jnp.concatenate([before, shard, after], axis=dim)
    return shard


def passed_along(block, axis, distance):
    devices = range(lax.axis_size(axis))
    route = [((i - distance) % len(devices), i) for i in devices]
    return lax.ppermute(block, axis, route)


def extend(field):
    halfway = lax.axis_size("lon") // 2
    widened = with_halo(field, (("lon", 1),), 1, True)
    banded = with_halo(widened, (("lat", 0),), 1, False)
    distant = passed_along(jnp.stack([widened[0], widened[-1]]), "lon", halfway)
    return (banded, distant)


def exchange(block, axis, bit):
    peers = lax.axis_size(axis)
    return lax.ppermute(block, axis, [(i, i ^ (1 << bit)) for i in range(peers)])


def butterfly_order():
    lat_bits = (lax.axis_size("lat") - 1).bit_length()
    lon_bits = (lax.axis_size("lon") - 1).bit_length()
    order = [("lat", b) for b in range(lat_bits)] + [("lon", b) for b in range(lon_bits)]
    return order


def butterfly_sum(value):
    value = jnp.sum(lax.all_gather(value, "lat"), 0)
    for bit in range((lax.axis_size("lon") - 1).bit_length()):
        value = value + exchange(value, "lon", bit)
    return value


def lon_halving_sum(rows):
    for bit in reversed(range((lax.axis_size("lon") - 1).bit_length())):
        half = rows.shape[1] // 2
        mine = (lax.axis_index("lon") >> bit) & 1
        keep = lax.dynamic_slice_in_dim(rows, mine * half, half, axis=1)
        send = lax.dynamic_slice_in_dim(rows, (1 - mine) * half, half, axis=1)
        rows = keep + exchange(send, "lon", bit)
    return rows


def conv_valid(field, weights):
    return lax.conv_general_dilated(
        field[None],
        weights,
        (1, 1),
        "VALID",
        dimension_numbers=("NHWC", "HWIO", "NHWC"),
        preferred_element_type=jnp.float32,
    )[0]


def local(fields, kernel, norm_gain, norm_shift, cotangent):
    height, breadth, channels = fields.shape
    north = lax.axis_index("lat") == 0
    south = lax.axis_index("lat") == lax.axis_size("lat") - 1
    banded, distant = extend(fields)
    merged = banded.at[0].set(jnp.where(north, distant[0], banded[0]))
    merged = merged.at[-1].set(jnp.where(south, distant[1], merged[-1]))
    conv_out = conv_valid(merged, kernel).reshape(-1, channels)
    count = height * breadth * lax.axis_size("lat") * lax.axis_size("lon") * (channels // G)
    local_stats = jnp.concatenate(
        [jnp.sum(conv_out, 0).reshape(G, -1).sum(1), jnp.sum(conv_out * conv_out, 0).reshape(G, -1).sum(1)]
    )
    stats = butterfly_sum(local_stats)
    mean = stats[:G] / count
    var = stats[G:] / count - mean * mean
    rstd = lax.rsqrt(var + 1e-05)
    mean_ch = jnp.repeat(mean, channels // G)
    rstd_ch = jnp.repeat(rstd, channels // G)
    ghat = (conv_out - mean_ch) * rstd_ch
    pre = ghat * norm_gain + norm_shift
    sigma = jax.nn.sigmoid(pre)
    block_out = (
        (fields.reshape(-1, channels).astype(jnp.float32) + pre * sigma)
        .astype(jnp.bfloat16)
        .reshape(height, breadth, channels)
    )
    upstream = cotangent.astype(jnp.float32).reshape(-1, channels)
    dpre = upstream * (sigma * (1.0 + pre * (1.0 - sigma)))
    grad_sums = butterfly_sum(jnp.concatenate([jnp.sum(dpre * ghat, 0), jnp.sum(dpre, 0)]))
    grad_gain, grad_shift = grad_sums[:channels], grad_sums[channels:]
    mean_a = (norm_gain * grad_shift).reshape(G, -1).sum(1) / count
    mean_b = (norm_gain * grad_gain).reshape(G, -1).sum(1) / count
    dconv = (
        (
            dpre * norm_gain
            - jnp.repeat(mean_a, channels // G)
            - ghat * jnp.repeat(mean_b, channels // G)
        )
        * rstd_ch
    ).astype(jnp.bfloat16)
    dconv = dconv.reshape(height, breadth, channels)
    grad_rows = dconv.reshape(-1, channels)
    taps = []
    for tap_row in range(3):
        for tap_col in range(3):
            shifted = merged[:, tap_col : tap_col + breadth].reshape(-1, channels)
            window = lax.slice_in_dim(shifted, tap_row * breadth, tap_row * breadth + height * breadth)
            taps.append(
                lax.dot_general(
                    grad_rows, window, (((0,), (0,)), ((), ())), preferred_element_type=jnp.float32
                )
            )
    owned_taps = lax.psum_scatter(jnp.stack(taps), "lat", scatter_dimension=1, tiled=True)
    owned_cols = owned_taps.transpose(1, 0, 2).reshape(owned_taps.shape[1], 9 * channels)
    grad_banded, grad_distant = extend(dconv)
    flipped = jnp.swapaxes(kernel[::-1, ::-1], 2, 3)
    back = conv_valid(grad_banded, flipped)
    upper_term = jnp.zeros((breadth, channels), jnp.float32)
    lower_term = jnp.zeros((breadth, channels), jnp.float32)
    for tap_col in range(3):
        upper_term = upper_term + jnp.dot(
            grad_distant[0, 2 - tap_col : 2 - tap_col + breadth],
            kernel[0, tap_col].T,
            preferred_element_type=jnp.float32,
        )
        lower_term = lower_term + jnp.dot(
            grad_distant[1, 2 - tap_col : 2 - tap_col + breadth],
            kernel[2, tap_col].T,
            preferred_element_type=jnp.float32,
        )
    back = back.at[0].add(jnp.where(north, upper_term, 0.0))
    back = back.at[-1].add(jnp.where(south, lower_term, 0.0))
    grad_fields = (upstream.reshape(height, breadth, channels) + back).astype(jnp.bfloat16)
    grad_kernel = lon_halving_sum(owned_cols).T
    return (block_out, grad_fields, grad_kernel, grad_gain, grad_shift)


def solution(mesh):
    in_specs = (P("lat", "lon", None), P(), P(), P(), P("lat", "lon", None))
    out_specs = (P("lat", "lon", None), P("lat", "lon", None), P("lon", "lat"), P(), P())
    return jax.shard_map(local, mesh=mesh, in_specs=in_specs, out_specs=out_specs, check_vma=False)
```

```python
import jax
import jax.numpy as jnp
from jax import lax
from jax.sharding import PartitionSpec as P

G = 32


def with_halo(shard, sides, width, wrap):
    for axis, dim in sides:
        peers, length = (lax.axis_size(axis), shard.shape[dim])
        up = [(i, (i + 1) % peers) for i in range(peers if wrap else peers - 1)]
        down = [(j, i) for i, j in up]
        last = lax.slice_in_dim(shard, length - width, length, axis=dim)
        initial = lax.slice_in_dim(shard, 0, width, axis=dim)
        if width == 1:
            before = jnp.expand_dims(lax.ppermute(jnp.squeeze(last, dim), axis, up), dim)
            if wrap:
                before, initial = lax.optimization_barrier((before, initial))
            after = jnp.expand_dims(lax.ppermute(jnp.squeeze(initial, dim), axis, down), dim)
        else:
            before = lax.ppermute(last, axis, up)
            after = lax.ppermute(initial, axis, down)
        shard = jnp.concatenate([before, shard, after], axis=dim)
    return shard


def passed_along(block, axis, distance):
    devices = range(lax.axis_size(axis))
    route = [((i - distance) % len(devices), i) for i in devices]
    return lax.ppermute(block, axis, route)


def extend(field):
    halfway = lax.axis_size("lon") // 2
    widened = with_halo(field, (("lon", 1),), 1, True)
    banded = with_halo(widened, (("lat", 0),), 1, False)
    distant = passed_along(jnp.stack([widened[0], widened[-1]]), "lon", halfway)
    return (banded, distant)


def exchange(block, axis, bit):
    peers = lax.axis_size(axis)
    return lax.ppermute(block, axis, [(i, i ^ (1 << bit)) for i in range(peers)])


def butterfly_order():
    lat_bits = (lax.axis_size("lat") - 1).bit_length()
    lon_bits = (lax.axis_size("lon") - 1).bit_length()
    order = [("lat", b) for b in range(lat_bits)] + [("lon", b) for b in range(lon_bits)]
    return order


def butterfly_sum(value):
    value = jnp.sum(lax.all_gather(value, "lat"), 0)
    for bit in range((lax.axis_size("lon") - 1).bit_length()):
        value = value + exchange(value, "lon", bit)
    return value


def lon_halving_sum(rows):
    for bit in reversed(range((lax.axis_size("lon") - 1).bit_length())):
        half = rows.shape[1] // 2
        mine = (lax.axis_index("lon") >> bit) & 1
        keep = lax.dynamic_slice_in_dim(rows, mine * half, half, axis=1)
        send = lax.dynamic_slice_in_dim(rows, (1 - mine) * half, half, axis=1)
        rows = keep + exchange(send, "lon", bit)
    return rows


def conv_valid(field, weights):
    return lax.conv_general_dilated(
        field[None],
        weights,
        (1, 1),
        "VALID",
        dimension_numbers=("NHWC", "HWIO", "NHWC"),
        preferred_element_type=jnp.float32,
    )[0]


def local(fields, kernel, norm_gain, norm_shift, cotangent):
    height, breadth, channels = fields.shape
    north = lax.axis_index("lat") == 0
    south = lax.axis_index("lat") == lax.axis_size("lat") - 1
    banded, distant = extend(fields)
    merged = banded.at[0].set(jnp.where(north, distant[0], banded[0]))
    merged = merged.at[-1].set(jnp.where(south, distant[1], merged[-1]))
    conv_out = conv_valid(merged, kernel).reshape(-1, channels)
    count = height * breadth * lax.axis_size("lat") * lax.axis_size("lon") * (channels // G)
    local_stats = jnp.concatenate(
        [jnp.sum(conv_out, 0).reshape(G, -1).sum(1), jnp.sum(conv_out * conv_out, 0).reshape(G, -1).sum(1)]
    )
    stats = butterfly_sum(local_stats)
    mean = stats[:G] / count
    var = stats[G:] / count - mean * mean
    rstd = lax.rsqrt(var + 1e-05)
    mean_ch = jnp.repeat(mean, channels // G)
    rstd_ch = jnp.repeat(rstd, channels // G)
    ghat = (conv_out - mean_ch) * rstd_ch
    pre = ghat * norm_gain + norm_shift
    sigma = jax.nn.sigmoid(pre)
    block_out = (
        (fields.reshape(-1, channels).astype(jnp.float32) + pre * sigma)
        .astype(jnp.bfloat16)
        .reshape(height, breadth, channels)
    )
    upstream = cotangent.astype(jnp.float32).reshape(-1, channels)
    dpre = upstream * (sigma * (1.0 + pre * (1.0 - sigma)))
    grad_sums = butterfly_sum(jnp.concatenate([jnp.sum(dpre * ghat, 0), jnp.sum(dpre, 0)]))
    grad_gain, grad_shift = grad_sums[:channels], grad_sums[channels:]
    mean_a = (norm_gain * grad_shift).reshape(G, -1).sum(1) / count
    mean_b = (norm_gain * grad_gain).reshape(G, -1).sum(1) / count
    dconv = (
        (
            dpre * norm_gain
            - jnp.repeat(mean_a, channels // G)
            - ghat * jnp.repeat(mean_b, channels // G)
        )
        * rstd_ch
    ).astype(jnp.bfloat16)
    dconv = dconv.reshape(height, breadth, channels)
    term = lax.conv_general_dilated(
        merged[None],
        dconv.reshape(height, breadth, 1, channels),
        (1, 1),
        "VALID",
        dimension_numbers=("CHWN", "HWIO", "CHWN"),
        preferred_element_type=jnp.float32,
    )
    owned_cols = lax.psum_scatter(term, "lat", scatter_dimension=0, tiled=True)
    owned_cols = owned_cols.reshape(owned_cols.shape[0], 9 * channels)
    grad_banded, grad_distant = extend(dconv)
    flipped = jnp.swapaxes(kernel[::-1, ::-1], 2, 3)
    back = conv_valid(grad_banded, flipped)
    upper_term = jnp.zeros((breadth, channels), jnp.float32)
    lower_term = jnp.zeros((breadth, channels), jnp.float32)
    for tap_col in range(3):
        upper_term = upper_term + jnp.dot(
            grad_distant[0, 2 - tap_col : 2 - tap_col + breadth],
            kernel[0, tap_col].T,
            preferred_element_type=jnp.float32,
        )
        lower_term = lower_term + jnp.dot(
            grad_distant[1, 2 - tap_col : 2 - tap_col + breadth],
            kernel[2, tap_col].T,
            preferred_element_type=jnp.float32,
        )
    back = back.at[0].add(jnp.where(north, upper_term, 0.0))
    back = back.at[-1].add(jnp.where(south, lower_term, 0.0))
    grad_fields = (upstream.reshape(height, breadth, channels) + back).astype(jnp.bfloat16)
    grad_kernel = lon_halving_sum(owned_cols).T
    return (block_out, grad_fields, grad_kernel, grad_gain, grad_shift)


def solution(mesh):
    in_specs = (P("lat", "lon", None), P(), P(), P(), P("lat", "lon", None))
    out_specs = (P("lat", "lon", None), P("lat", "lon", None), P("lon", "lat"), P(), P())
    return jax.shard_map(local, mesh=mesh, in_specs=in_specs, out_specs=out_specs, check_vma=False)
```

```python
import jax
import jax.numpy as jnp
from jax import lax
from jax.sharding import PartitionSpec as P

G = 32


def with_halo(shard, sides, width, wrap):
    for axis, dim in sides:
        peers, length = (lax.axis_size(axis), shard.shape[dim])
        up = [(i, (i + 1) % peers) for i in range(peers if wrap else peers - 1)]
        down = [(j, i) for i, j in up]
        last = lax.slice_in_dim(shard, length - width, length, axis=dim)
        initial = lax.slice_in_dim(shard, 0, width, axis=dim)
        if width == 1:
            before = jnp.expand_dims(lax.ppermute(jnp.squeeze(last, dim), axis, up), dim)
            after = jnp.expand_dims(lax.ppermute(jnp.squeeze(initial, dim), axis, down), dim)
        else:
            before = lax.ppermute(last, axis, up)
            after = lax.ppermute(initial, axis, down)
        shard = jnp.concatenate([before, shard, after], axis=dim)
    return shard


def passed_along(block, axis, distance):
    devices = range(lax.axis_size(axis))
    route = [((i - distance) % len(devices), i) for i in devices]
    return lax.ppermute(block, axis, route)


def extend(field):
    halfway = lax.axis_size("lon") // 2
    widened = with_halo(field, (("lon", 1),), 1, True)
    banded = with_halo(widened, (("lat", 0),), 1, False)
    distant = passed_along(jnp.stack([widened[0], widened[-1]]), "lon", halfway)
    return (banded, distant)


def exchange(block, axis, bit):
    peers = lax.axis_size(axis)
    return lax.ppermute(block, axis, [(i, i ^ (1 << bit)) for i in range(peers)])


def butterfly_order():
    lat_bits = (lax.axis_size("lat") - 1).bit_length()
    lon_bits = (lax.axis_size("lon") - 1).bit_length()
    order = [("lat", b) for b in range(lat_bits)] + [("lon", b) for b in range(lon_bits)]
    return order


def butterfly_sum(value):
    value = jnp.sum(lax.all_gather(value, "lat"), 0)
    for bit in range((lax.axis_size("lon") - 1).bit_length()):
        value = value + exchange(value, "lon", bit)
    return value


def lon_halving_sum(rows):
    for bit in reversed(range((lax.axis_size("lon") - 1).bit_length())):
        half = rows.shape[1] // 2
        mine = (lax.axis_index("lon") >> bit) & 1
        keep = lax.dynamic_slice_in_dim(rows, mine * half, half, axis=1)
        send = lax.dynamic_slice_in_dim(rows, (1 - mine) * half, half, axis=1)
        rows = keep + exchange(send, "lon", bit)
    return rows


def conv_valid(field, weights):
    return lax.conv_general_dilated(
        field[None],
        weights,
        (1, 1),
        "VALID",
        dimension_numbers=("NHWC", "HWIO", "NHWC"),
        preferred_element_type=jnp.float32,
    )[0]


def local(fields, kernel, norm_gain, norm_shift, cotangent):
    height, breadth, channels = fields.shape
    north = lax.axis_index("lat") == 0
    south = lax.axis_index("lat") == lax.axis_size("lat") - 1
    banded, distant = extend(fields)
    merged = banded.at[0].set(jnp.where(north, distant[0], banded[0]))
    merged = merged.at[-1].set(jnp.where(south, distant[1], merged[-1]))
    conv_out = conv_valid(merged, kernel).reshape(-1, channels)
    count = height * breadth * lax.axis_size("lat") * lax.axis_size("lon") * (channels // G)
    local_stats = jnp.concatenate(
        [jnp.sum(conv_out, 0).reshape(G, -1).sum(1), jnp.sum(conv_out * conv_out, 0).reshape(G, -1).sum(1)]
    )
    stats = butterfly_sum(jnp.pad(local_stats, (0, 2 * channels - 2 * G)))[: 2 * G]
    mean = stats[:G] / count
    var = stats[G:] / count - mean * mean
    rstd = lax.rsqrt(var + 1e-05)
    mean_ch = jnp.repeat(mean, channels // G)
    rstd_ch = jnp.repeat(rstd, channels // G)
    ghat = (conv_out - mean_ch) * rstd_ch
    pre = ghat * norm_gain + norm_shift
    sigma = jax.nn.sigmoid(pre)
    block_out = (
        (fields.reshape(-1, channels).astype(jnp.float32) + pre * sigma)
        .astype(jnp.bfloat16)
        .reshape(height, breadth, channels)
    )
    upstream = cotangent.astype(jnp.float32).reshape(-1, channels)
    dpre = upstream * (sigma * (1.0 + pre * (1.0 - sigma)))
    grad_sums = butterfly_sum(jnp.concatenate([jnp.sum(dpre * ghat, 0), jnp.sum(dpre, 0)]))
    grad_gain, grad_shift = grad_sums[:channels], grad_sums[channels:]
    mean_a = (norm_gain * grad_shift).reshape(G, -1).sum(1) / count
    mean_b = (norm_gain * grad_gain).reshape(G, -1).sum(1) / count
    dconv = (
        (
            dpre * norm_gain
            - jnp.repeat(mean_a, channels // G)
            - ghat * jnp.repeat(mean_b, channels // G)
        )
        * rstd_ch
    ).astype(jnp.bfloat16)
    dconv = dconv.reshape(height, breadth, channels)
    term = lax.conv_general_dilated(
        merged[None],
        dconv.reshape(height, breadth, 1, channels),
        (1, 1),
        "VALID",
        dimension_numbers=("CHWN", "HWIO", "CHWN"),
        preferred_element_type=jnp.float32,
    )
    owned_cols = lax.psum_scatter(term, "lat", scatter_dimension=0, tiled=True)
    owned_cols = owned_cols.reshape(owned_cols.shape[0], 9 * channels)
    grad_banded, grad_distant = extend(dconv)
    flipped = jnp.swapaxes(kernel[::-1, ::-1], 2, 3)
    back = conv_valid(grad_banded, flipped)
    upper_term = jnp.zeros((breadth, channels), jnp.float32)
    lower_term = jnp.zeros((breadth, channels), jnp.float32)
    for tap_col in range(3):
        upper_term = upper_term + jnp.dot(
            grad_distant[0, 2 - tap_col : 2 - tap_col + breadth],
            kernel[0, tap_col].T,
            preferred_element_type=jnp.float32,
        )
        lower_term = lower_term + jnp.dot(
            grad_distant[1, 2 - tap_col : 2 - tap_col + breadth],
            kernel[2, tap_col].T,
            preferred_element_type=jnp.float32,
        )
    back = back.at[0].add(jnp.where(north, upper_term, 0.0))
    back = back.at[-1].add(jnp.where(south, lower_term, 0.0))
    grad_fields = (upstream.reshape(height, breadth, channels) + back).astype(jnp.bfloat16)
    grad_kernel = lon_halving_sum(owned_cols).T
    return (block_out, grad_fields, grad_kernel, grad_gain, grad_shift)


def solution(mesh):
    in_specs = (P("lat", "lon", None), P(), P(), P(), P("lat", "lon", None))
    out_specs = (P("lat", "lon", None), P("lat", "lon", None), P("lon", "lat"), P(), P())
    return jax.shard_map(local, mesh=mesh, in_specs=in_specs, out_specs=out_specs, check_vma=False)
```
